256 devices in a mesh: blk: 64 (over z, x_lo, y), circ: 4 (over x_hi, core).
Axes of the slice: x: 4 (x_hi: 2, x_lo: 2; x = x_hi * 2 + x_lo), y: 4, z: 8, core: 2. Of those that a mesh axis runs over, the one named last changes fastest.
Arguments:
- panels: float32 [4, 8192], P(None, ('blk', 'circ')), may hold values from -2 to 2, as said below
- node_of_panel: int32 [8192], P(('blk', 'circ')), may hold values from 0 to 2047, as said below
- stiffener_rows: int32 [32], replicated, may hold values from 0 to 511
- density_start: float32 [16, 8192], P(None, ('blk', 'circ')), may hold values from -6 to 6
- motion_start: float32 [16, 512, 1024], P(None, 'blk', 'circ'), may hold values from -6 to 6
- force: float32 [16, 512, 1024], P(None, 'blk', 'circ'), may hold values from -128 to 128
- stiffness: float32 [512, 1024], P('blk', 'circ'), may hold values from 0.5 to 2
Outputs:
- source_density: float32 [16, 8192], P(None, ('blk', 'circ'))
- surface_pressure: float32 [16, 8192], P(None, ('blk', 'circ'))
- shell_motion: float32 [16, 512, 1024], P(None, 'blk', 'circ')
The draws below stay inside these ranges and needn't reach their ends.
Inputs may be any that keep to these rules, and one draw needn't show every extreme that they name: `panels`: every panel lies between 0.98 and 1.02 from the z axis, with z between -2 and 2 and area between 0.5 and 2 times 8 pi / 8192. `node_of_panel`: counted as row * 256 + column within the tile of the device that holds the panel. `stiffener_rows`: A row may be listed more than once.
All inputs are finite; a program needn't handle non-finite values.
Results may differ from the reference program's by a relative error of at most 0.0029.
Values may be sent and summed in bfloat16 or wider, within the bound.
No kernel may reach another device: no remote copies, remote signals or barrier semaphores. Data moves between devices by JAX's collectives and lax.ppermute only.
A program may use at most 64 MiB of HBM per device.

```python
import math
import jax
import jax.numpy as jnp
from jax import lax

PD = 32
SA = 8
SC = 256
LOADS = 8
ITERS = 4
SWEEPS = 2
PANELS = 8192
NA = 512
NC = 1024
HOOPS = 32
N_CIRC = 4


def panel_nodes(key):
    return jax.random.randint(jax.random.fold_in(key, 11), (PANELS,), 0, SA * SC, dtype=jnp.int32)


def draw_node_of_panel(key, part):
    return panel_nodes(key)


def draw_panels(key, part):
    nodes = panel_nodes(key)
    device_of = jnp.arange(PANELS, dtype=jnp.int32) // PD
    circ_count = NC // SC
    node_row = device_of // circ_count * SA + nodes // SC
    node_col = device_of % circ_count * SC + nodes % SC
    keys = jax.random.split(jax.random.fold_in(key, 23), 4)
    axial_jitter = jax.random.uniform(keys[0], (PANELS,), jnp.float32)
    angle_jitter = jax.random.uniform(keys[1], (PANELS,), jnp.float32)
    radial_jitter = 2.0 * jax.random.uniform(keys[2], (PANELS,), jnp.float32) - 1.0
    area_jitter = jax.random.uniform(keys[3], (PANELS,), jnp.float32)
    height = (node_row.astype(jnp.float32) + axial_jitter) * (4.0 / NA) - 2.0
    angle = (node_col.astype(jnp.float32) + angle_jitter) * (2.0 * math.pi / NC)
    radius = 1.0 + 0.02 * radial_jitter
    areas = 8.0 * math.pi / PANELS * jnp.exp(math.log(0.5) + math.log(4.0) * area_jitter)
    return jnp.stack([radius * jnp.cos(angle), radius * jnp.sin(angle), height, areas], axis=0)


def place_ends(array, key, low, high):
    shape = array.shape
    index_at = [jax.random.randint(jax.random.fold_in(key, axis), (), 0, shape[axis]) for axis in range(len(shape))]
    array = array.at[tuple(index_at)].set(low)
    longest = shape.index(max(shape))
    index_at[longest] = (index_at[longest] + 1) % shape[longest]
    return array.at[tuple(index_at)].set(high)


def block_levels(key, shape, shards, least, top_value):
    def one(position, blocks):
        heights = jax.random.uniform(jax.random.fold_in(jax.random.fold_in(key, 6), position), (blocks,), jnp.float32, least / len(shards), top_value / len(shards))
        return jnp.repeat(jnp.exp(heights), shape[position] // blocks).reshape((-1,) + (1,) * (len(shape) - position - 1))

    factor_of = one(*shards[0])
    for cut in shards[1:]:
        factor_of = factor_of * one(*cut)
    return factor_of


def centred(rng, dims, deviation, bound, shards=(), held_as=jnp.bfloat16):
    values = jax.random.normal(rng, dims, jnp.float32) * deviation
    if len(shards) > 0:
        values = block_levels(rng, dims, shards, -0.22, 0.18) * values
    return jnp.clip(values, min=-bound, max=bound).astype(held_as)


def setup_inputs(seed: int = 0) -> dict:
    streams_of = jax.random.split(jax.random.key(seed), 8)
    panels = draw_panels(jax.random.fold_in(streams_of[7], 71), 0)
    node_of_panel = draw_node_of_panel(jax.random.fold_in(streams_of[7], 71), 0)
    stiffener_rows = place_ends(jax.random.randint(streams_of[2], (HOOPS,), 0, NA), jax.random.fold_in(streams_of[2], 1), 0, NA - 1).astype(jnp.int32)
    density_start = centred(streams_of[3], (2 * LOADS, PANELS), 1.0, 6.0, ((1, 256),), jnp.float32)
    motion_start = centred(streams_of[4], (2 * LOADS, NA, NC), 1.0, 6.0, ((1, 64), (2, 4)), jnp.float32)
    force = centred(streams_of[5], (2 * LOADS, NA, NC), 20.0, 128.0, ((1, 64), (2, 4)), jnp.float32)
    stiffness = jnp.clip(jnp.exp(math.log(2.0) - 1.3862944 * jax.random.uniform(streams_of[6], (NA, NC), jnp.float32) ** block_levels(streams_of[6], (NA, NC), ((0, 64), (1, 4)), -0.2, 0.2)), 0.5, 2.0)
    return {"panels": panels, "node_of_panel": node_of_panel, "stiffener_rows": stiffener_rows, "density_start": density_start, "motion_start": motion_start, "force": force, "stiffness": stiffness}


wave_number = 4.0
single_scale = 30.0
double_scale = 6.0
hoop_spring = 40.0
inertia_term = 4.0
loss_factor = 0.2
relaxation = 0.3

def kernel_blocks(targets, sources):
    radial = jnp.sqrt(targets[0] * targets[0] + targets[1] * targets[1])
    normal_x = (targets[0] / radial)[:, None]
    normal_y = (targets[1] / radial)[:, None]
    delta_x = targets[0][:, None] - sources[0][None, :]
    delta_y = targets[1][:, None] - sources[1][None, :]
    delta_z = targets[2][:, None] - sources[2][None, :]
    areas = sources[3][None, :]
    dist_sq = delta_x * delta_x + delta_y * delta_y + delta_z * delta_z + areas / math.pi
    distance = jnp.sqrt(dist_sq)
    inverse = 1.0 / distance
    phase_arg = wave_number * distance
    cosine = jnp.cos(phase_arg)
    sine_part = jnp.sin(phase_arg)
    weight = areas * (1.0 / (4.0 * math.pi)) * inverse
    single = single_scale * weight
    double = double_scale * weight * (normal_x * delta_x + normal_y * delta_y) * inverse * inverse
    real_stack = jnp.concatenate([single * cosine, double * (-cosine - phase_arg * sine_part)], axis=0)
    imag_stack = jnp.concatenate([single * sine_part, double * (phase_arg * cosine - sine_part)], axis=0)
    return (real_stack.astype(jnp.bfloat16), imag_stack.astype(jnp.bfloat16))

def laplace_full(field):
    widths = [(0, 0)] * (field.ndim - 2) + [(1, 1), (0, 0)]
    padded = jnp.pad(field, widths)
    return padded[..., 2:, :] + padded[..., :-2, :] + jnp.roll(field, 1, axis=-1) + jnp.roll(field, -1, axis=-1) - 4.0 * field

def relax(motion, bend, load, stiffness, hoop_rows):
    half = motion.shape[0] // 2
    shift = hoop_spring * hoop_rows - inertia_term
    applied_re = bend[:half] - loss_factor * bend[half:] + shift * motion[:half]
    applied_im = bend[half:] + loss_factor * bend[:half] + shift * motion[half:]
    resid_re = load[:half] - applied_re
    resid_im = load[half:] - applied_im
    diag_re = 20.0 * stiffness + shift
    diag_im = 20.0 * loss_factor * stiffness
    denom = diag_re * diag_re + diag_im * diag_im
    update_re = (resid_re * diag_re + resid_im * diag_im) / denom
    update_im = (resid_im * diag_re - resid_re * diag_im) / denom
    return motion + relaxation * jnp.concatenate([update_re, update_im], axis=0)

def reference(panels, node_of_panel, stiffener_rows, density_start, motion_start, force, stiffness):
    panel_count = panels.shape[1]
    channels = density_start.shape[0]
    half = channels // 2
    axial_rows = motion_start.shape[1]
    columns = motion_start.shape[2]
    device_of = jnp.arange(panel_count, dtype=jnp.int32) // PD
    blk_of = device_of // N_CIRC
    circ_of = device_of % N_CIRC
    node_row = blk_of * SA + node_of_panel // SC
    node_col = circ_of * SC + node_of_panel % SC
    node_flat = (node_row * columns + node_col).astype(jnp.int32)
    hoop_rows = jnp.any(jnp.arange(axial_rows, dtype=jnp.int32)[:, None] == stiffener_rows[None, :], axis=1)
    hoop_rows = hoop_rows.astype(jnp.float32)[:, None]
    panel_weight = panels[3] * (panel_count / (8.0 * math.pi))
    row_block = math.gcd(panel_count, 256)
    block_count = panel_count // row_block
    target_blocks = jnp.transpose(panels.reshape(4, block_count, row_block), (1, 0, 2))
    density = density_start
    motion = motion_start
    pressure = jnp.zeros_like(density_start)
    for round_index in range(ITERS):
        neumann = motion.reshape(channels, axial_rows * columns)[:, node_flat]
        density_bf = lax.optimization_barrier(density.astype(jnp.bfloat16)).astype(jnp.float32)
        rotated = jnp.concatenate([-density_bf[half:], density_bf[:half]], axis=0)

        def apply_rows(target_block):
            real_stack, imag_stack = kernel_blocks(target_block, panels)
            real_f = lax.optimization_barrier(real_stack).astype(jnp.float32)
            imag_f = lax.optimization_barrier(imag_stack).astype(jnp.float32)
            first = jnp.einsum('lc,rc->lr', density_bf, real_f, precision=lax.Precision.HIGHEST)
            second = jnp.einsum('lc,rc->lr', rotated, imag_f, precision=lax.Precision.HIGHEST)
            return first + second
        results = lax.map(apply_rows, target_blocks)
        single_part = jnp.transpose(results[:, :, :row_block], (1, 0, 2)).reshape(channels, panel_count)
        double_part = jnp.transpose(results[:, :, row_block:], (1, 0, 2)).reshape(channels, panel_count)
        pressure = single_part
        density = 0.5 * density + neumann - double_part
        fluid = jnp.zeros((channels, axial_rows * columns), jnp.float32)
        fluid = fluid.at[:, node_flat].add(panel_weight[None, :] * pressure)
        load = force - fluid.reshape(channels, axial_rows, columns)
        for sweep_index in range(SWEEPS):
            bend = laplace_full(stiffness * laplace_full(motion))
            motion = relax(motion, bend, load, stiffness, hoop_rows)
    return (density, pressure, motion)
```

```python
import math

import jax
import jax.numpy as jnp
from jax import lax
from jax.sharding import PartitionSpec as P

ITERS = 4
SWEEPS = 2


wave_number = 4.0
single_scale = 30.0
double_scale = 6.0
hoop_spring = 40.0
inertia_term = 4.0
loss_factor = 0.2
relaxation = 0.3


def gather_columns(block):
    count = lax.axis_size("blk") * lax.axis_size("circ")
    index = lax.axis_index("blk") * lax.axis_size("circ") + lax.axis_index("circ")
    held = block[None]
    bit = 1
    while bit < count:
        pairs = [(i, i ^ bit) for i in range(count)]
        other = lax.ppermute(held, ("blk", "circ"), pairs)
        low = (index & bit) == 0
        first = jnp.where(low, held, other)
        second = jnp.where(low, other, held)
        held = jnp.concatenate([first, second], axis=0)
        bit *= 2
    return jnp.transpose(held, (1, 0, 2)).reshape(block.shape[0], count * block.shape[1])


def laplace_halo(field):
    rows = lax.axis_size("blk")
    cols = lax.axis_size("circ")
    above = lax.ppermute(field[:, -1:, :], "blk", [(i, i + 1) for i in range(rows - 1)])
    below = lax.ppermute(field[:, :1, :], "blk", [(i + 1, i) for i in range(rows - 1)])
    left = lax.ppermute(field[:, :, -1:], "circ", [(i, (i + 1) % cols) for i in range(cols)])
    right = lax.ppermute(field[:, :, :1], "circ", [(i, (i - 1) % cols) for i in range(cols)])
    down = jnp.concatenate([field[:, 1:, :], below], axis=1)
    up = jnp.concatenate([above, field[:, :-1, :]], axis=1)
    east = jnp.concatenate([field[:, :, 1:], right], axis=2)
    west = jnp.concatenate([left, field[:, :, :-1]], axis=2)
    return down + up + east + west - 4.0 * field


def kernel_blocks(targets, sources):
    radial = jnp.sqrt(targets[0] * targets[0] + targets[1] * targets[1])
    normal_x = (targets[0] / radial)[:, None]
    normal_y = (targets[1] / radial)[:, None]
    delta_x = targets[0][:, None] - sources[0][None, :]
    delta_y = targets[1][:, None] - sources[1][None, :]
    delta_z = targets[2][:, None] - sources[2][None, :]
    areas = sources[3][None, :]
    dist_sq = delta_x * delta_x + delta_y * delta_y + delta_z * delta_z + areas / math.pi
    distance = jnp.sqrt(dist_sq)
    inverse = 1.0 / distance
    phase_arg = wave_number * distance
    cosine = jnp.cos(phase_arg)
    sine_part = jnp.sin(phase_arg)
    weight = areas * (1.0 / (4.0 * math.pi)) * inverse
    single = single_scale * weight
    double = double_scale * weight * (normal_x * delta_x + normal_y * delta_y) * inverse * inverse
    real_stack = jnp.concatenate(
        [single * cosine, double * (-cosine - phase_arg * sine_part)], axis=0
    )
    imag_stack = jnp.concatenate(
        [single * sine_part, double * (phase_arg * cosine - sine_part)], axis=0
    )
    return (real_stack.astype(jnp.bfloat16), imag_stack.astype(jnp.bfloat16))


def form_kernels(targets, sources):
    width = sources.shape[1]
    block_cols = math.gcd(width, 1024)
    block_count = width // block_cols
    source_blocks = jnp.transpose(sources.reshape(4, block_count, block_cols), (1, 0, 2))
    real_blocks, imag_blocks = lax.map(lambda block: kernel_blocks(targets, block), source_blocks)
    rows_out = real_blocks.shape[1]
    real_stack = jnp.transpose(real_blocks, (1, 0, 2)).reshape(rows_out, width)
    imag_stack = jnp.transpose(imag_blocks, (1, 0, 2)).reshape(rows_out, width)
    return (real_stack, imag_stack)


def fold_columns(real_stack, imag_stack):

    def fold_step(running, shard_piece, first_col):
        half = shard_piece.shape[0] // 2
        rotated = jnp.concatenate([-shard_piece[half:], shard_piece[:half]], axis=0)
        first = jnp.einsum("lc,rc->lr", shard_piece, real_stack, preferred_element_type=jnp.float32)
        second = jnp.einsum("lc,rc->lr", rotated, imag_stack, preferred_element_type=jnp.float32)
        return first + second

    return fold_step


def relax(motion, bend, load, stiffness, hoop_rows):
    half = motion.shape[0] // 2
    shift = hoop_spring * hoop_rows - inertia_term
    applied_re = bend[:half] - loss_factor * bend[half:] + shift * motion[:half]
    applied_im = bend[half:] + loss_factor * bend[:half] + shift * motion[half:]
    resid_re = load[:half] - applied_re
    resid_im = load[half:] - applied_im
    diag_re = 20.0 * stiffness + shift
    diag_im = 20.0 * loss_factor * stiffness
    denom = diag_re * diag_re + diag_im * diag_im
    update_re = (resid_re * diag_re + resid_im * diag_im) / denom
    update_im = (resid_im * diag_re - resid_re * diag_im) / denom
    return motion + relaxation * jnp.concatenate([update_re, update_im], axis=0)


def per_device(
    panels, node_of_panel, stiffener_rows, density_start, motion_start, force, stiffness
):
    panel_dev = panels.shape[1]
    channels = density_start.shape[0]
    axial, circum = stiffness.shape
    blk_index = lax.axis_index("blk")
    devices = lax.axis_size("blk") * lax.axis_size("circ")
    rows_global = blk_index * axial + jnp.arange(axial, dtype=jnp.int32)
    hoop_rows = jnp.any(rows_global[:, None] == stiffener_rows[None, :], axis=1).astype(
        jnp.float32
    )[:, None]
    panel_weight = panels[3] * (panel_dev * devices / (8.0 * math.pi))
    sources = gather_columns(panels)
    target_rows = panels.shape[1]
    real_stack, imag_stack = form_kernels(panels, sources)
    fold_step = fold_columns(real_stack, imag_stack)
    density = density_start
    motion = motion_start
    pressure = jnp.zeros_like(density_start)
    for round_index in range(ITERS):
        flat_motion = motion.reshape(channels, axial * circum)
        neumann = jnp.take(flat_motion, node_of_panel, axis=1)
        density_bf = density.astype(jnp.bfloat16)
        start_sum = jnp.zeros((channels, 2 * target_rows), jnp.float32)
        combined = fold_step(
            start_sum, gather_columns(density_bf), jnp.int32(0)
        )
        single_part = combined[:, :target_rows]
        double_part = combined[:, target_rows:]
        pressure = single_part
        density = 0.5 * density + neumann - double_part
        fluid = jnp.zeros((channels, axial * circum), jnp.float32)
        fluid = fluid.at[:, node_of_panel].add(panel_weight[None, :] * pressure)
        load = force - fluid.reshape(channels, axial, circum)
        for sweep_index in range(SWEEPS):
            moment = stiffness * laplace_halo(motion)
            bend = laplace_halo(moment)
            motion = relax(motion, bend, load, stiffness, hoop_rows)
    return (density, pressure, motion)


def solution(mesh):
    in_specs = (
        P(None, ("blk", "circ")),
        P(("blk", "circ")),
        P(),
        P(None, ("blk", "circ")),
        P(None, "blk", "circ"),
        P(None, "blk", "circ"),
        P("blk", "circ"),
    )
    out_specs = (P(None, ("blk", "circ")), P(None, ("blk", "circ")), P(None, "blk", "circ"))
    return jax.shard_map(
        per_device, mesh=mesh, in_specs=in_specs, out_specs=out_specs, check_vma=False
    )
```

```python
import math

import jax
import jax.numpy as jnp
from jax import lax
from jax.sharding import PartitionSpec as P

ITERS = 4
SWEEPS = 2


wave_number = 4.0
single_scale = 30.0
double_scale = 6.0
hoop_spring = 40.0
inertia_term = 4.0
loss_factor = 0.2
relaxation = 0.3


def gather_columns(block):
    count = lax.axis_size("blk") * lax.axis_size("circ")
    index = lax.axis_index("blk") * lax.axis_size("circ") + lax.axis_index("circ")
    held = block[None]
    bit = 1
    while bit < count:
        pairs = [(i, i ^ bit) for i in range(count)]
        other = lax.ppermute(held, ("blk", "circ"), pairs)
        low = (index & bit) == 0
        first = jnp.where(low, held, other)
        second = jnp.where(low, other, held)
        held = jnp.concatenate([first, second], axis=0)
        bit *= 2
    return jnp.transpose(held, (1, 0, 2)).reshape(block.shape[0], count * block.shape[1])


def with_halo(field, width):
    rows = lax.axis_size("blk")
    cols = lax.axis_size("circ")
    above = lax.ppermute(field[:, -width:, :], "blk", [(i, i + 1) for i in range(rows - 1)])
    below = lax.ppermute(field[:, :width, :], "blk", [(i + 1, i) for i in range(rows - 1)])
    field = jnp.concatenate([above, field, below], axis=1)
    left = lax.ppermute(field[:, :, -width:], "circ", [(i, (i + 1) % cols) for i in range(cols)])
    right = lax.ppermute(field[:, :, :width], "circ", [(i, (i - 1) % cols) for i in range(cols)])
    return jnp.concatenate([left, field, right], axis=2)


def laplace_inner(extended):
    return (
        extended[..., 2:, 1:-1]
        + extended[..., :-2, 1:-1]
        + extended[..., 1:-1, 2:]
        + extended[..., 1:-1, :-2]
        - 4.0 * extended[..., 1:-1, 1:-1]
    )


def trim(field, width):
    return field[..., width:field.shape[-2] - width, width:field.shape[-1] - width]


def kernel_blocks(targets, sources):
    radial = jnp.sqrt(targets[0] * targets[0] + targets[1] * targets[1])
    normal_x = (targets[0] / radial)[:, None]
    normal_y = (targets[1] / radial)[:, None]
    delta_x = targets[0][:, None] - sources[0][None, :]
    delta_y = targets[1][:, None] - sources[1][None, :]
    delta_z = targets[2][:, None] - sources[2][None, :]
    areas = sources[3][None, :]
    dist_sq = delta_x * delta_x + delta_y * delta_y + delta_z * delta_z + areas / math.pi
    distance = jnp.sqrt(dist_sq)
    inverse = 1.0 / distance
    phase_arg = wave_number * distance
    cosine = jnp.cos(phase_arg)
    sine_part = jnp.sin(phase_arg)
    weight = areas * (1.0 / (4.0 * math.pi)) * inverse
    single = single_scale * weight
    double = double_scale * weight * (normal_x * delta_x + normal_y * delta_y) * inverse * inverse
    real_stack = jnp.concatenate(
        [single * cosine, double * (-cosine - phase_arg * sine_part)], axis=0
    )
    imag_stack = jnp.concatenate(
        [single * sine_part, double * (phase_arg * cosine - sine_part)], axis=0
    )
    return (real_stack.astype(jnp.bfloat16), imag_stack.astype(jnp.bfloat16))


def form_kernels(targets, sources):
    width = sources.shape[1]
    block_cols = math.gcd(width, 1024)
    block_count = width // block_cols
    source_blocks = jnp.transpose(sources.reshape(4, block_count, block_cols), (1, 0, 2))
    real_blocks, imag_blocks = lax.map(lambda block: kernel_blocks(targets, block), source_blocks)
    rows_out = real_blocks.shape[1]
    real_stack = jnp.transpose(real_blocks, (1, 0, 2)).reshape(rows_out, width)
    imag_stack = jnp.transpose(imag_blocks, (1, 0, 2)).reshape(rows_out, width)
    return (real_stack, imag_stack)


def fold_columns(real_stack, imag_stack):

    def fold_step(running, shard_piece, first_col):
        half = shard_piece.shape[0] // 2
        rotated = jnp.concatenate([-shard_piece[half:], shard_piece[:half]], axis=0)
        first = jnp.einsum("lc,rc->lr", shard_piece, real_stack, preferred_element_type=jnp.float32)
        second = jnp.einsum("lc,rc->lr", rotated, imag_stack, preferred_element_type=jnp.float32)
        return first + second

    return fold_step


def relax(motion, bend, load, stiffness, hoop_rows):
    half = motion.shape[0] // 2
    shift = hoop_spring * hoop_rows - inertia_term
    applied_re = bend[:half] - loss_factor * bend[half:] + shift * motion[:half]
    applied_im = bend[half:] + loss_factor * bend[:half] + shift * motion[half:]
    resid_re = load[:half] - applied_re
    resid_im = load[half:] - applied_im
    diag_re = 20.0 * stiffness + shift
    diag_im = 20.0 * loss_factor * stiffness
    denom = diag_re * diag_re + diag_im * diag_im
    update_re = (resid_re * diag_re + resid_im * diag_im) / denom
    update_im = (resid_im * diag_re - resid_re * diag_im) / denom
    return motion + relaxation * jnp.concatenate([update_re, update_im], axis=0)


def per_device(
    panels, node_of_panel, stiffener_rows, density_start, motion_start, force, stiffness
):
    panel_dev = panels.shape[1]
    channels = density_start.shape[0]
    axial, circum = stiffness.shape
    width = 2 * SWEEPS
    blk_index = lax.axis_index("blk")
    devices = lax.axis_size("blk") * lax.axis_size("circ")
    total_rows = axial * lax.axis_size("blk")
    rows_global = blk_index * axial - width + jnp.arange(axial + 2 * width, dtype=jnp.int32)
    inside = ((rows_global >= 0) & (rows_global < total_rows))[:, None]
    hoop_rows = jnp.any(rows_global[:, None] == stiffener_rows[None, :], axis=1).astype(
        jnp.float32
    )[:, None]
    panel_weight = panels[3] * (panel_dev * devices / (8.0 * math.pi))
    joined = gather_columns(jnp.concatenate([panels, density_start], axis=0))
    sources = joined[:4]
    target_rows = panels.shape[1]
    real_stack, imag_stack = form_kernels(panels, sources)
    fold_step = fold_columns(real_stack, imag_stack)
    density = density_start
    motion = motion_start
    pressure = jnp.zeros_like(density_start)
    for round_index in range(ITERS):
        flat_motion = motion.reshape(channels, axial * circum)
        neumann = jnp.take(flat_motion, node_of_panel, axis=1)
        density_bf = density.astype(jnp.bfloat16)
        if round_index == 0:
            gathered = joined[4:].astype(jnp.bfloat16)
        else:
            gathered = gather_columns(density_bf)
        start_sum = jnp.zeros((channels, 2 * target_rows), jnp.float32)
        combined = fold_step(start_sum, gathered, jnp.int32(0))
        single_part = combined[:, :target_rows]
        double_part = combined[:, target_rows:]
        pressure = single_part
        density = 0.5 * density + neumann - double_part
        fluid = jnp.zeros((channels, axial * circum), jnp.float32)
        fluid = fluid.at[:, node_of_panel].add(panel_weight[None, :] * pressure)
        load = force - fluid.reshape(channels, axial, circum)
        state = with_halo(jnp.concatenate([motion, load, stiffness[None]], axis=0), width)
        motion_ext = state[:channels]
        load_ext = state[channels:2 * channels]
        stiff_ext = state[2 * channels]
        for sweep_index in range(SWEEPS):
            edge = 2 * sweep_index + 1
            moment = trim(stiff_ext, edge) * laplace_inner(motion_ext)
            moment = jnp.where(inside[edge:inside.shape[0] - edge], moment, 0.0)
            bend = laplace_inner(moment)
            edge += 1
            rows_at = slice(edge, inside.shape[0] - edge)
            motion_ext = relax(
                trim(motion_ext, 2), bend, trim(load_ext, edge), trim(stiff_ext, edge), hoop_rows[rows_at]
            )
            motion_ext = jnp.where(inside[rows_at], motion_ext, 0.0)
        motion = motion_ext
    return (density, pressure, motion)


def solution(mesh):
    in_specs = (
        P(None, ("blk", "circ")),
        P(("blk", "circ")),
        P(),
        P(None, ("blk", "circ")),
        P(None, "blk", "circ"),
        P(None, "blk", "circ"),
        P("blk", "circ"),
    )
    out_specs = (P(None, ("blk", "circ")), P(None, ("blk", "circ")), P(None, "blk", "circ"))
    return jax.shard_map(
        per_device, mesh=mesh, in_specs=in_specs, out_specs=out_specs, check_vma=False
    )
```

```python
import math

import jax
import jax.numpy as jnp
from jax import lax
from jax.sharding import PartitionSpec as P

ITERS = 4
SWEEPS = 2


wave_number = 4.0
single_scale = 30.0
double_scale = 6.0
hoop_spring = 40.0
inertia_term = 4.0
loss_factor = 0.2
relaxation = 0.3


def gather_columns(block):
    count = lax.axis_size("blk") * lax.axis_size("circ")
    index = lax.axis_index("blk") * lax.axis_size("circ") + lax.axis_index("circ")
    bits = count.bit_length() - 1
    held = block
    for level in reversed(range(bits)):
        bit = 1 << level
        pairs = [(i, i ^ bit) for i in range(count)]
        other = lax.ppermute(held, ("blk", "circ"), pairs)
        low = (index & bit) == 0
        first = jnp.where(low, held, other)
        second = jnp.where(low, other, held)
        held = jnp.stack([first, second], axis=0)
    order = list(reversed(range(bits)))
    held = jnp.transpose(held, order + [bits, bits + 1])
    held = held.reshape((count,) + block.shape)
    return jnp.transpose(held, (1, 0, 2)).reshape(block.shape[0], count * block.shape[1])


def with_halo(field, width):
    rows = lax.axis_size("blk")
    cols = lax.axis_size("circ")
    above = lax.ppermute(field[:, -width:, :], "blk", [(i, i + 1) for i in range(rows - 1)])
    below = lax.ppermute(field[:, :width, :], "blk", [(i + 1, i) for i in range(rows - 1)])
    field = jnp.concatenate([above, field, below], axis=1)
    left = lax.ppermute(field[:, :, -width:], "circ", [(i, (i + 1) % cols) for i in range(cols)])
    right = lax.ppermute(field[:, :, :width], "circ", [(i, (i - 1) % cols) for i in range(cols)])
    return jnp.concatenate([left, field, right], axis=2)


def laplace_inner(extended):
    return (
        extended[..., 2:, 1:-1]
        + extended[..., :-2, 1:-1]
        + extended[..., 1:-1, 2:]
        + extended[..., 1:-1, :-2]
        - 4.0 * extended[..., 1:-1, 1:-1]
    )


def trim(field, width):
    return field[..., width:field.shape[-2] - width, width:field.shape[-1] - width]


def kernel_blocks(targets, sources):
    radial = jnp.sqrt(targets[0] * targets[0] + targets[1] * targets[1])
    normal_x = (targets[0] / radial)[:, None]
    normal_y = (targets[1] / radial)[:, None]
    delta_x = targets[0][:, None] - sources[0][None, :]
    delta_y = targets[1][:, None] - sources[1][None, :]
    delta_z = targets[2][:, None] - sources[2][None, :]
    areas = sources[3][None, :]
    dist_sq = delta_x * delta_x + delta_y * delta_y + delta_z * delta_z + areas / math.pi
    distance = jnp.sqrt(dist_sq)
    inverse = 1.0 / distance
    phase_arg = wave_number * distance
    cosine = jnp.cos(phase_arg)
    sine_part = jnp.sin(phase_arg)
    weight = areas * (1.0 / (4.0 * math.pi)) * inverse
    single = single_scale * weight
    double = double_scale * weight * (normal_x * delta_x + normal_y * delta_y) * inverse * inverse
    real_stack = jnp.concatenate(
        [single * cosine, double * (-cosine - phase_arg * sine_part)], axis=0
    )
    imag_stack = jnp.concatenate(
        [single * sine_part, double * (phase_arg * cosine - sine_part)], axis=0
    )
    return (real_stack.astype(jnp.bfloat16), imag_stack.astype(jnp.bfloat16))


def form_kernels(targets, sources):
    width = sources.shape[1]
    block_cols = width
    block_count = width // block_cols
    source_blocks = jnp.transpose(sources.reshape(4, block_count, block_cols), (1, 0, 2))
    real_blocks, imag_blocks = lax.map(lambda block: kernel_blocks(targets, block), source_blocks)
    rows_out = real_blocks.shape[1]
    real_stack = jnp.transpose(real_blocks, (1, 0, 2)).reshape(rows_out, width)
    imag_stack = jnp.transpose(imag_blocks, (1, 0, 2)).reshape(rows_out, width)
    return (real_stack, imag_stack)


def fold_columns(real_stack, imag_stack):

    def fold_step(running, shard_piece, first_col):
        half = shard_piece.shape[0] // 2
        rotated = jnp.concatenate([-shard_piece[half:], shard_piece[:half]], axis=0)
        first = jnp.einsum("lc,rc->lr", shard_piece, real_stack, preferred_element_type=jnp.float32)
        second = jnp.einsum("lc,rc->lr", rotated, imag_stack, preferred_element_type=jnp.float32)
        return first + second

    return fold_step


def relax(motion, bend, load, stiffness, hoop_rows):
    half = motion.shape[0] // 2
    shift = hoop_spring * hoop_rows - inertia_term
    applied_re = bend[:half] - loss_factor * bend[half:] + shift * motion[:half]
    applied_im = bend[half:] + loss_factor * bend[:half] + shift * motion[half:]
    resid_re = load[:half] - applied_re
    resid_im = load[half:] - applied_im
    diag_re = 20.0 * stiffness + shift
    diag_im = 20.0 * loss_factor * stiffness
    denom = diag_re * diag_re + diag_im * diag_im
    update_re = (resid_re * diag_re + resid_im * diag_im) / denom
    update_im = (resid_im * diag_re - resid_re * diag_im) / denom
    return motion + relaxation * jnp.concatenate([update_re, update_im], axis=0)


def per_device(
    panels, node_of_panel, stiffener_rows, density_start, motion_start, force, stiffness
):
    panel_dev = panels.shape[1]
    channels = density_start.shape[0]
    axial, circum = stiffness.shape
    width = 2 * SWEEPS
    blk_index = lax.axis_index("blk")
    devices = lax.axis_size("blk") * lax.axis_size("circ")
    total_rows = axial * lax.axis_size("blk")
    rows_global = blk_index * axial - width + jnp.arange(axial + 2 * width, dtype=jnp.int32)
    inside = ((rows_global >= 0) & (rows_global < total_rows))[:, None]
    hoop_rows = jnp.any(rows_global[:, None] == stiffener_rows[None, :], axis=1).astype(
        jnp.float32
    )[:, None]
    panel_weight = panels[3] * (panel_dev * devices / (8.0 * math.pi))
    joined = gather_columns(jnp.concatenate([panels, density_start], axis=0))
    sources = joined[:4]
    target_rows = panels.shape[1]
    real_stack, imag_stack = form_kernels(panels, sources)
    fold_step = fold_columns(real_stack, imag_stack)
    density = density_start
    motion = motion_start
    pressure = jnp.zeros_like(density_start)
    for round_index in range(ITERS):
        flat_motion = motion.reshape(channels, axial * circum)
        neumann = jnp.take(flat_motion, node_of_panel, axis=1)
        density_bf = density.astype(jnp.bfloat16)
        if round_index == 0:
            gathered = joined[4:].astype(jnp.bfloat16)
        else:
            gathered = gather_columns(density_bf)
        start_sum = jnp.zeros((channels, 2 * target_rows), jnp.float32)
        combined = fold_step(start_sum, gathered, jnp.int32(0))
        single_part = combined[:, :target_rows]
        double_part = combined[:, target_rows:]
        pressure = single_part
        density = 0.5 * density + neumann - double_part
        fluid = jnp.zeros((channels, axial * circum), jnp.float32)
        fluid = fluid.at[:, node_of_panel].add(panel_weight[None, :] * pressure)
        load = force - fluid.reshape(channels, axial, circum)
        state = with_halo(jnp.concatenate([motion, load, stiffness[None]], axis=0), width)
        motion_ext = state[:channels]
        load_ext = state[channels:2 * channels]
        stiff_ext = state[2 * channels]
        for sweep_index in range(SWEEPS):
            edge = 2 * sweep_index + 1
            moment = trim(stiff_ext, edge) * laplace_inner(motion_ext)
            moment = jnp.where(inside[edge:inside.shape[0] - edge], moment, 0.0)
            bend = laplace_inner(moment)
            edge += 1
            rows_at = slice(edge, inside.shape[0] - edge)
            motion_ext = relax(
                trim(motion_ext, 2), bend, trim(load_ext, edge), trim(stiff_ext, edge), hoop_rows[rows_at]
            )
            motion_ext = jnp.where(inside[rows_at], motion_ext, 0.0)
        motion = motion_ext
    return (density, pressure, motion)


def solution(mesh):
    in_specs = (
        P(None, ("blk", "circ")),
        P(("blk", "circ")),
        P(),
        P(None, ("blk", "circ")),
        P(None, "blk", "circ"),
        P(None, "blk", "circ"),
        P("blk", "circ"),
    )
    out_specs = (P(None, ("blk", "circ")), P(None, ("blk", "circ")), P(None, "blk", "circ"))
    return jax.shard_map(
        per_device, mesh=mesh, in_specs=in_specs, out_specs=out_specs, check_vma=False
    )
```

```python
import math

import jax
import jax.numpy as jnp
from jax import lax
from jax.sharding import PartitionSpec as P

ITERS = 4
SWEEPS = 2


wave_number = 4.0
single_scale = 30.0
double_scale = 6.0
hoop_spring = 40.0
inertia_term = 4.0
loss_factor = 0.2
relaxation = 0.3


def gather_columns(block):
    count = lax.axis_size("blk") * lax.axis_size("circ")
    bits = count.bit_length() - 1
    held = block
    for level in reversed(range(bits)):
        bit = 1 << level
        pairs = [(i, i ^ bit) for i in range(count)]
        other = lax.ppermute(held, ("blk", "circ"), pairs)
        held = jnp.stack([held, other], axis=0)
    order = list(reversed(range(bits)))
    held = jnp.transpose(held, order + [bits, bits + 1])
    held = held.reshape((count,) + block.shape)
    return jnp.transpose(held, (1, 0, 2)).reshape(block.shape[0], count * block.shape[1])


def with_halo(field, width):
    rows = lax.axis_size("blk")
    cols = lax.axis_size("circ")
    above = lax.ppermute(field[:, -width:, :], "blk", [(i, i + 1) for i in range(rows - 1)])
    below = lax.ppermute(field[:, :width, :], "blk", [(i + 1, i) for i in range(rows - 1)])
    field = jnp.concatenate([above, field, below], axis=1)
    left = lax.ppermute(field[:, :, -width:], "circ", [(i, (i + 1) % cols) for i in range(cols)])
    right = lax.ppermute(field[:, :, :width], "circ", [(i, (i - 1) % cols) for i in range(cols)])
    return jnp.concatenate([left, field, right], axis=2)


def laplace_inner(extended):
    return (
        extended[..., 2:, 1:-1]
        + extended[..., :-2, 1:-1]
        + extended[..., 1:-1, 2:]
        + extended[..., 1:-1, :-2]
        - 4.0 * extended[..., 1:-1, 1:-1]
    )


def trim(field, width):
    return field[..., width:field.shape[-2] - width, width:field.shape[-1] - width]


def kernel_blocks(targets, sources):
    radial = jnp.sqrt(targets[0] * targets[0] + targets[1] * targets[1])
    normal_x = (targets[0] / radial)[:, None]
    normal_y = (targets[1] / radial)[:, None]
    delta_x = targets[0][:, None] - sources[0][None, :]
    delta_y = targets[1][:, None] - sources[1][None, :]
    delta_z = targets[2][:, None] - sources[2][None, :]
    areas = sources[3][None, :]
    dist_sq = delta_x * delta_x + delta_y * delta_y + delta_z * delta_z + areas / math.pi
    distance = jnp.sqrt(dist_sq)
    inverse = 1.0 / distance
    phase_arg = wave_number * distance
    cosine = jnp.cos(phase_arg)
    sine_part = jnp.sin(phase_arg)
    weight = areas * (1.0 / (4.0 * math.pi)) * inverse
    single = single_scale * weight
    double = double_scale * weight * (normal_x * delta_x + normal_y * delta_y) * inverse * inverse
    real_stack = jnp.concatenate(
        [single * cosine, double * (-cosine - phase_arg * sine_part)], axis=0
    )
    imag_stack = jnp.concatenate(
        [single * sine_part, double * (phase_arg * cosine - sine_part)], axis=0
    )
    return (real_stack.astype(jnp.bfloat16), imag_stack.astype(jnp.bfloat16))


def form_kernels(targets, sources):
    width = sources.shape[1]
    block_cols = width
    block_count = width // block_cols
    source_blocks = jnp.transpose(sources.reshape(4, block_count, block_cols), (1, 0, 2))
    real_blocks, imag_blocks = lax.map(lambda block: kernel_blocks(targets, block), source_blocks)
    rows_out = real_blocks.shape[1]
    real_stack = jnp.transpose(real_blocks, (1, 0, 2)).reshape(rows_out, width)
    imag_stack = jnp.transpose(imag_blocks, (1, 0, 2)).reshape(rows_out, width)
    return (real_stack, imag_stack)


def fold_columns(real_stack, imag_stack):

    def fold_step(running, shard_piece, first_col):
        half = shard_piece.shape[0] // 2
        rotated = jnp.concatenate([-shard_piece[half:], shard_piece[:half]], axis=0)
        first = jnp.einsum("lc,rc->lr", shard_piece, real_stack, preferred_element_type=jnp.float32)
        second = jnp.einsum("lc,rc->lr", rotated, imag_stack, preferred_element_type=jnp.float32)
        return first + second

    return fold_step


def relax(motion, bend, load, stiffness, hoop_rows):
    half = motion.shape[0] // 2
    shift = hoop_spring * hoop_rows - inertia_term
    applied_re = bend[:half] - loss_factor * bend[half:] + shift * motion[:half]
    applied_im = bend[half:] + loss_factor * bend[:half] + shift * motion[half:]
    resid_re = load[:half] - applied_re
    resid_im = load[half:] - applied_im
    diag_re = 20.0 * stiffness + shift
    diag_im = 20.0 * loss_factor * stiffness
    denom = diag_re * diag_re + diag_im * diag_im
    update_re = (resid_re * diag_re + resid_im * diag_im) / denom
    update_im = (resid_im * diag_re - resid_re * diag_im) / denom
    return motion + relaxation * jnp.concatenate([update_re, update_im], axis=0)


def per_device(
    panels, node_of_panel, stiffener_rows, density_start, motion_start, force, stiffness
):
    panel_dev = panels.shape[1]
    channels = density_start.shape[0]
    axial, circum = stiffness.shape
    width = 2 * SWEEPS
    blk_index = lax.axis_index("blk")
    devices = lax.axis_size("blk") * lax.axis_size("circ")
    total_rows = axial * lax.axis_size("blk")
    rows_global = blk_index * axial - width + jnp.arange(axial + 2 * width, dtype=jnp.int32)
    inside = ((rows_global >= 0) & (rows_global < total_rows))[:, None]
    hoop_rows = jnp.any(rows_global[:, None] == stiffener_rows[None, :], axis=1).astype(
        jnp.float32
    )[:, None]
    panel_weight = panels[3] * (panel_dev * devices / (8.0 * math.pi))
    joined = gather_columns(jnp.concatenate([panels, density_start], axis=0))
    sources = joined[:4]
    target_rows = panels.shape[1]
    real_stack, imag_stack = form_kernels(panels, sources)
    fold_step = fold_columns(real_stack, imag_stack)
    density = density_start
    motion = motion_start
    pressure = jnp.zeros_like(density_start)
    for round_index in range(ITERS):
        flat_motion = motion.reshape(channels, axial * circum)
        neumann = jnp.take(flat_motion, node_of_panel, axis=1)
        density_bf = density.astype(jnp.bfloat16)
        if round_index == 0:
            gathered = joined[4:].astype(jnp.bfloat16)
        else:
            gathered = gather_columns(density_bf)
        start_sum = jnp.zeros((channels, 2 * target_rows), jnp.float32)
        combined = fold_step(start_sum, gathered, jnp.int32(0))
        single_part = combined[:, :target_rows]
        double_part = combined[:, target_rows:]
        pressure = single_part
        density = 0.5 * density + neumann - double_part
        fluid = jnp.zeros((channels, axial * circum), jnp.float32)
        fluid = fluid.at[:, node_of_panel].add(panel_weight[None, :] * pressure)
        load = force - fluid.reshape(channels, axial, circum)
        state = with_halo(jnp.concatenate([motion, load, stiffness[None]], axis=0), width)
        motion_ext = state[:channels]
        load_ext = state[channels:2 * channels]
        stiff_ext = state[2 * channels]
        for sweep_index in range(SWEEPS):
            edge = 2 * sweep_index + 1
            moment = trim(stiff_ext, edge) * laplace_inner(motion_ext)
            moment = jnp.where(inside[edge:inside.shape[0] - edge], moment, 0.0)
            bend = laplace_inner(moment)
            edge += 1
            rows_at = slice(edge, inside.shape[0] - edge)
            motion_ext = relax(
                trim(motion_ext, 2), bend, trim(load_ext, edge), trim(stiff_ext, edge), hoop_rows[rows_at]
            )
            motion_ext = jnp.where(inside[rows_at], motion_ext, 0.0)
        motion = motion_ext
    return (density, pressure, motion)


def solution(mesh):
    in_specs = (
        P(None, ("blk", "circ")),
        P(("blk", "circ")),
        P(),
        P(None, ("blk", "circ")),
        P(None, "blk", "circ"),
        P(None, "blk", "circ"),
        P("blk", "circ"),
    )
    out_specs = (P(None, ("blk", "circ")), P(None, ("blk", "circ")), P(None, "blk", "circ"))
    return jax.shard_map(
        per_device, mesh=mesh, in_specs=in_specs, out_specs=out_specs, check_vma=False
    )
```

```python
import math

import jax
import jax.numpy as jnp
from jax import lax
from jax.sharding import PartitionSpec as P

ITERS = 4
SWEEPS = 2


wave_number = 4.0
single_scale = 30.0
double_scale = 6.0
hoop_spring = 40.0
inertia_term = 4.0
loss_factor = 0.2
relaxation = 0.3


def gather_columns(block):
    count = lax.axis_size("blk") * lax.axis_size("circ")
    bits = count.bit_length() - 1
    held = block
    for level in reversed(range(bits)):
        bit = 1 << level
        pairs = [(i, i ^ bit) for i in range(count)]
        other = lax.ppermute(held, ("blk", "circ"), pairs)
        held = jnp.stack([held, other], axis=0)
    order = list(reversed(range(bits)))
    held = jnp.transpose(held, order + [bits, bits + 1])
    held = held.reshape((count,) + block.shape)
    return jnp.transpose(held, (1, 0, 2)).reshape(block.shape[0], count * block.shape[1])


def with_halo(field, width):
    rows = lax.axis_size("blk")
    cols = lax.axis_size("circ")
    above = lax.ppermute(field[:, -width:, :], "blk", [(i, i + 1) for i in range(rows - 1)])
    below = lax.ppermute(field[:, :width, :], "blk", [(i + 1, i) for i in range(rows - 1)])
    field = jnp.concatenate([above, field, below], axis=1)
    left = lax.ppermute(field[:, :, -width:], "circ", [(i, (i + 1) % cols) for i in range(cols)])
    right = lax.ppermute(field[:, :, :width], "circ", [(i, (i - 1) % cols) for i in range(cols)])
    return jnp.concatenate([left, field, right], axis=2)


def laplace_inner(extended):
    return (
        extended[..., 2:, 1:-1]
        + extended[..., :-2, 1:-1]
        + extended[..., 1:-1, 2:]
        + extended[..., 1:-1, :-2]
        - 4.0 * extended[..., 1:-1, 1:-1]
    )


def trim(field, width):
    return field[..., width:field.shape[-2] - width, width:field.shape[-1] - width]


def kernel_blocks(targets, sources):
    radial = jnp.sqrt(targets[0] * targets[0] + targets[1] * targets[1])
    normal_x = (targets[0] / radial)[:, None]
    normal_y = (targets[1] / radial)[:, None]
    delta_x = targets[0][:, None] - sources[0][None, :]
    delta_y = targets[1][:, None] - sources[1][None, :]
    delta_z = targets[2][:, None] - sources[2][None, :]
    areas = sources[3][None, :]
    dist_sq = delta_x * delta_x + delta_y * delta_y + delta_z * delta_z + areas / math.pi
    distance = jnp.sqrt(dist_sq)
    inverse = 1.0 / distance
    phase_arg = wave_number * distance
    cosine = jnp.cos(phase_arg)
    sine_part = jnp.sin(phase_arg)
    weight = areas * (1.0 / (4.0 * math.pi)) * inverse
    single = single_scale * weight
    double = double_scale * weight * (normal_x * delta_x + normal_y * delta_y) * inverse * inverse
    real_stack = jnp.concatenate(
        [single * cosine, double * (-cosine - phase_arg * sine_part)], axis=0
    )
    imag_stack = jnp.concatenate(
        [single * sine_part, double * (phase_arg * cosine - sine_part)], axis=0
    )
    return (real_stack.astype(jnp.bfloat16), imag_stack.astype(jnp.bfloat16))


def form_kernels(targets, sources):
    width = sources.shape[1]
    block_cols = width
    block_count = width // block_cols
    source_blocks = jnp.transpose(sources.reshape(4, block_count, block_cols), (1, 0, 2))
    real_blocks, imag_blocks = lax.map(lambda block: kernel_blocks(targets, block), source_blocks)
    rows_out = real_blocks.shape[1]
    real_stack = jnp.transpose(real_blocks, (1, 0, 2)).reshape(rows_out, width)
    imag_stack = jnp.transpose(imag_blocks, (1, 0, 2)).reshape(rows_out, width)
    return (real_stack, imag_stack)


def fold_columns(real_stack, imag_stack):

    def fold_step(running, shard_piece, first_col):
        half = shard_piece.shape[0] // 2
        rotated = jnp.concatenate([-shard_piece[half:], shard_piece[:half]], axis=0)
        first = jnp.einsum("lc,rc->lr", shard_piece, real_stack, preferred_element_type=jnp.float32)
        second = jnp.einsum("lc,rc->lr", rotated, imag_stack, preferred_element_type=jnp.float32)
        return first + second

    return fold_step


def relax(motion, bend, load, stiffness, hoop_rows):
    half = motion.shape[0] // 2
    shift = hoop_spring * hoop_rows - inertia_term
    applied_re = bend[:half] - loss_factor * bend[half:] + shift * motion[:half]
    applied_im = bend[half:] + loss_factor * bend[:half] + shift * motion[half:]
    resid_re = load[:half] - applied_re
    resid_im = load[half:] - applied_im
    diag_re = 20.0 * stiffness + shift
    diag_im = 20.0 * loss_factor * stiffness
    denom = diag_re * diag_re + diag_im * diag_im
    update_re = (resid_re * diag_re + resid_im * diag_im) / denom
    update_im = (resid_im * diag_re - resid_re * diag_im) / denom
    return motion + relaxation * jnp.concatenate([update_re, update_im], axis=0)


def per_device(
    panels, node_of_panel, stiffener_rows, density_start, motion_start, force, stiffness
):
    panel_dev = panels.shape[1]
    channels = density_start.shape[0]
    axial, circum = stiffness.shape
    width = 2 * SWEEPS
    blk_index = lax.axis_index("blk")
    devices = lax.axis_size("blk") * lax.axis_size("circ")
    total_rows = axial * lax.axis_size("blk")
    rows_global = blk_index * axial - width + jnp.arange(axial + 2 * width, dtype=jnp.int32)
    inside = ((rows_global >= 0) & (rows_global < total_rows))[:, None]
    hoop_rows = jnp.any(rows_global[:, None] == stiffener_rows[None, :], axis=1).astype(
        jnp.float32
    )[:, None]
    panel_weight = panels[3] * (panel_dev * devices / (8.0 * math.pi))
    joined = gather_columns(jnp.concatenate([panels, density_start], axis=0))
    sources = joined[:4]
    target_rows = panels.shape[1]
    real_stack, imag_stack = form_kernels(panels, sources)
    fold_step = fold_columns(real_stack, imag_stack)
    def one_round(density, motion, gathered):
        flat_motion = motion.reshape(channels, axial * circum)
        neumann = jnp.take(flat_motion, node_of_panel, axis=1)
        start_sum = jnp.zeros((channels, 2 * target_rows), jnp.float32)
        combined = fold_step(start_sum, gathered, jnp.int32(0))
        single_part = combined[:, :target_rows]
        double_part = combined[:, target_rows:]
        pressure = single_part
        density = 0.5 * density + neumann - double_part
        fluid = jnp.zeros((channels, axial * circum), jnp.float32)
        fluid = fluid.at[:, node_of_panel].add(panel_weight[None, :] * pressure)
        load = force - fluid.reshape(channels, axial, circum)
        state = with_halo(jnp.concatenate([motion, load, stiffness[None]], axis=0), width)
        motion_ext = state[:channels]
        load_ext = state[channels:2 * channels]
        stiff_ext = state[2 * channels]
        for sweep_index in range(SWEEPS):
            edge = 2 * sweep_index + 1
            moment = trim(stiff_ext, edge) * laplace_inner(motion_ext)
            moment = jnp.where(inside[edge:inside.shape[0] - edge], moment, 0.0)
            bend = laplace_inner(moment)
            edge += 1
            rows_at = slice(edge, inside.shape[0] - edge)
            motion_ext = relax(
                trim(motion_ext, 2), bend, trim(load_ext, edge), trim(stiff_ext, edge), hoop_rows[rows_at]
            )
            motion_ext = jnp.where(inside[rows_at], motion_ext, 0.0)
        return density, motion_ext, pressure

    density, motion, pressure = one_round(
        density_start, motion_start, joined[4:].astype(jnp.bfloat16)
    )

    def later_round(_, carried):
        density, motion, pressure = carried
        return one_round(density, motion, gather_columns(density.astype(jnp.bfloat16)))

    density, motion, pressure = lax.fori_loop(1, ITERS, later_round, (density, motion, pressure))
    return (density, pressure, motion)


def solution(mesh):
    in_specs = (
        P(None, ("blk", "circ")),
        P(("blk", "circ")),
        P(),
        P(None, ("blk", "circ")),
        P(None, "blk", "circ"),
        P(None, "blk", "circ"),
        P("blk", "circ"),
    )
    out_specs = (P(None, ("blk", "circ")), P(None, ("blk", "circ")), P(None, "blk", "circ"))
    return jax.shard_map(
        per_device, mesh=mesh, in_specs=in_specs, out_specs=out_specs, check_vma=False
    )
```

```python
import math

import jax
import jax.numpy as jnp
from jax import lax
from jax.sharding import PartitionSpec as P

ITERS = 4
SWEEPS = 2


wave_number = 4.0
single_scale = 30.0
double_scale = 6.0
hoop_spring = 40.0
inertia_term = 4.0
loss_factor = 0.2
relaxation = 0.3


def gather_columns(block):
    count = lax.axis_size("blk") * lax.axis_size("circ")
    bits = count.bit_length() - 1
    held = block
    for level in reversed(range(bits)):
        bit = 1 << level
        pairs = [(i, i ^ bit) for i in range(count)]
        other = lax.ppermute(held, ("blk", "circ"), pairs)
        held = jnp.stack([held, other], axis=0)
    order = list(reversed(range(bits)))
    held = jnp.transpose(held, order + [bits, bits + 1])
    held = held.reshape((count,) + block.shape)
    return jnp.transpose(held, (1, 0, 2)).reshape(block.shape[0], count * block.shape[1])


def with_halo(field, width):
    rows = lax.axis_size("blk")
    cols = lax.axis_size("circ")
    both = ("blk", "circ")

    def diagonal(piece, step_row, step_col):
        pairs = [
            (b * cols + c, (b + step_row) * cols + (c + step_col) % cols)
            for b in range(rows)
            for c in range(cols)
            if 0 <= b + step_row < rows
        ]
        return lax.ppermute(piece, both, pairs)

    above = lax.ppermute(field[:, -width:, :], "blk", [(i, i + 1) for i in range(rows - 1)])
    below = lax.ppermute(field[:, :width, :], "blk", [(i + 1, i) for i in range(rows - 1)])
    left = lax.ppermute(field[:, :, -width:], "circ", [(i, (i + 1) % cols) for i in range(cols)])
    right = lax.ppermute(field[:, :, :width], "circ", [(i, (i - 1) % cols) for i in range(cols)])
    upper_left = diagonal(field[:, -width:, -width:], 1, 1)
    upper_right = diagonal(field[:, -width:, :width], 1, -1)
    lower_left = diagonal(field[:, :width, -width:], -1, 1)
    lower_right = diagonal(field[:, :width, :width], -1, -1)
    top = jnp.concatenate([upper_left, above, upper_right], axis=2)
    middle = jnp.concatenate([left, field, right], axis=2)
    bottom = jnp.concatenate([lower_left, below, lower_right], axis=2)
    return jnp.concatenate([top, middle, bottom], axis=1)


def laplace_inner(extended):
    return (
        extended[..., 2:, 1:-1]
        + extended[..., :-2, 1:-1]
        + extended[..., 1:-1, 2:]
        + extended[..., 1:-1, :-2]
        - 4.0 * extended[..., 1:-1, 1:-1]
    )


def trim(field, width):
    return field[..., width:field.shape[-2] - width, width:field.shape[-1] - width]


def kernel_blocks(targets, sources):
    radial = jnp.sqrt(targets[0] * targets[0] + targets[1] * targets[1])
    normal_x = (targets[0] / radial)[:, None]
    normal_y = (targets[1] / radial)[:, None]
    delta_x = targets[0][:, None] - sources[0][None, :]
    delta_y = targets[1][:, None] - sources[1][None, :]
    delta_z = targets[2][:, None] - sources[2][None, :]
    areas = sources[3][None, :]
    dist_sq = delta_x * delta_x + delta_y * delta_y + delta_z * delta_z + areas / math.pi
    distance = jnp.sqrt(dist_sq)
    inverse = 1.0 / distance
    phase_arg = wave_number * distance
    cosine = jnp.cos(phase_arg)
    sine_part = jnp.sin(phase_arg)
    weight = areas * (1.0 / (4.0 * math.pi)) * inverse
    single = single_scale * weight
    double = double_scale * weight * (normal_x * delta_x + normal_y * delta_y) * inverse * inverse
    real_stack = jnp.concatenate(
        [single * cosine, double * (-cosine - phase_arg * sine_part)], axis=0
    )
    imag_stack = jnp.concatenate(
        [single * sine_part, double * (phase_arg * cosine - sine_part)], axis=0
    )
    return (real_stack.astype(jnp.bfloat16), imag_stack.astype(jnp.bfloat16))


def form_kernels(targets, sources):
    width = sources.shape[1]
    block_cols = width
    block_count = width // block_cols
    source_blocks = jnp.transpose(sources.reshape(4, block_count, block_cols), (1, 0, 2))
    real_blocks, imag_blocks = lax.map(lambda block: kernel_blocks(targets, block), source_blocks)
    rows_out = real_blocks.shape[1]
    real_stack = jnp.transpose(real_blocks, (1, 0, 2)).reshape(rows_out, width)
    imag_stack = jnp.transpose(imag_blocks, (1, 0, 2)).reshape(rows_out, width)
    return (real_stack, imag_stack)


def fold_columns(real_stack, imag_stack):

    def fold_step(running, shard_piece, first_col):
        half = shard_piece.shape[0] // 2
        rotated = jnp.concatenate([-shard_piece[half:], shard_piece[:half]], axis=0)
        first = jnp.einsum("lc,rc->lr", shard_piece, real_stack, preferred_element_type=jnp.float32)
        second = jnp.einsum("lc,rc->lr", rotated, imag_stack, preferred_element_type=jnp.float32)
        return first + second

    return fold_step


def relax(motion, bend, load, stiffness, hoop_rows):
    half = motion.shape[0] // 2
    shift = hoop_spring * hoop_rows - inertia_term
    applied_re = bend[:half] - loss_factor * bend[half:] + shift * motion[:half]
    applied_im = bend[half:] + loss_factor * bend[:half] + shift * motion[half:]
    resid_re = load[:half] - applied_re
    resid_im = load[half:] - applied_im
    diag_re = 20.0 * stiffness + shift
    diag_im = 20.0 * loss_factor * stiffness
    denom = diag_re * diag_re + diag_im * diag_im
    update_re = (resid_re * diag_re + resid_im * diag_im) / denom
    update_im = (resid_im * diag_re - resid_re * diag_im) / denom
    return motion + relaxation * jnp.concatenate([update_re, update_im], axis=0)


def per_device(
    panels, node_of_panel, stiffener_rows, density_start, motion_start, force, stiffness
):
    panel_dev = panels.shape[1]
    channels = density_start.shape[0]
    axial, circum = stiffness.shape
    width = 2 * SWEEPS
    blk_index = lax.axis_index("blk")
    devices = lax.axis_size("blk") * lax.axis_size("circ")
    total_rows = axial * lax.axis_size("blk")
    rows_global = blk_index * axial - width + jnp.arange(axial + 2 * width, dtype=jnp.int32)
    inside = ((rows_global >= 0) & (rows_global < total_rows))[:, None]
    hoop_rows = jnp.any(rows_global[:, None] == stiffener_rows[None, :], axis=1).astype(
        jnp.float32
    )[:, None]
    panel_weight = panels[3] * (panel_dev * devices / (8.0 * math.pi))
    joined = gather_columns(jnp.concatenate([panels, density_start], axis=0))
    sources = joined[:4]
    target_rows = panels.shape[1]
    real_stack, imag_stack = form_kernels(panels, sources)
    fold_step = fold_columns(real_stack, imag_stack)
    density = density_start
    motion = motion_start
    pressure = jnp.zeros_like(density_start)
    for round_index in range(ITERS):
        flat_motion = motion.reshape(channels, axial * circum)
        neumann = jnp.take(flat_motion, node_of_panel, axis=1)
        density_bf = density.astype(jnp.bfloat16)
        if round_index == 0:
            gathered = joined[4:].astype(jnp.bfloat16)
        else:
            gathered = gather_columns(density_bf)
        start_sum = jnp.zeros((channels, 2 * target_rows), jnp.float32)
        combined = fold_step(start_sum, gathered, jnp.int32(0))
        single_part = combined[:, :target_rows]
        double_part = combined[:, target_rows:]
        pressure = single_part
        density = 0.5 * density + neumann - double_part
        fluid = jnp.zeros((channels, axial * circum), jnp.float32)
        fluid = fluid.at[:, node_of_panel].add(panel_weight[None, :] * pressure)
        load = force - fluid.reshape(channels, axial, circum)
        state = with_halo(jnp.concatenate([motion, load, stiffness[None]], axis=0), width)
        motion_ext = state[:channels]
        load_ext = state[channels:2 * channels]
        stiff_ext = state[2 * channels]
        for sweep_index in range(SWEEPS):
            edge = 2 * sweep_index + 1
            moment = trim(stiff_ext, edge) * laplace_inner(motion_ext)
            moment = jnp.where(inside[edge:inside.shape[0] - edge], moment, 0.0)
            bend = laplace_inner(moment)
            edge += 1
            rows_at = slice(edge, inside.shape[0] - edge)
            motion_ext = relax(
                trim(motion_ext, 2), bend, trim(load_ext, edge), trim(stiff_ext, edge), hoop_rows[rows_at]
            )
            motion_ext = jnp.where(inside[rows_at], motion_ext, 0.0)
        motion = motion_ext
    return (density, pressure, motion)


def solution(mesh):
    in_specs = (
        P(None, ("blk", "circ")),
        P(("blk", "circ")),
        P(),
        P(None, ("blk", "circ")),
        P(None, "blk", "circ"),
        P(None, "blk", "circ"),
        P("blk", "circ"),
    )
    out_specs = (P(None, ("blk", "circ")), P(None, ("blk", "circ")), P(None, "blk", "circ"))
    return jax.shard_map(
        per_device, mesh=mesh, in_specs=in_specs, out_specs=out_specs, check_vma=False
    )
```

```python
import math

import jax
import jax.numpy as jnp
from jax import lax
from jax.sharding import PartitionSpec as P

ITERS = 4
SWEEPS = 2


wave_number = 4.0
single_scale = 30.0
double_scale = 6.0
hoop_spring = 40.0
inertia_term = 4.0
loss_factor = 0.2
relaxation = 0.3


def gather_columns(block):
    count = lax.axis_size("blk") * lax.axis_size("circ")
    bits = count.bit_length() - 1
    held = block
    levels = list(reversed(range(bits)))
    if bits == 8:
        levels = [7, 6, 1, 5, 4, 3, 2, 0]
    for level in levels:
        bit = 1 << level
        pairs = [(i, i ^ bit) for i in range(count)]
        other = lax.ppermute(held, ("blk", "circ"), pairs)
        held = jnp.stack([held, other], axis=0)
    order = [bits - 1 - levels.index(bits - 1 - j) for j in range(bits)]
    held = jnp.transpose(held, order + [bits, bits + 1])
    held = held.reshape((count,) + block.shape)
    return jnp.transpose(held, (1, 0, 2)).reshape(block.shape[0], count * block.shape[1])


def with_halo(field, width):
    rows = lax.axis_size("blk")
    cols = lax.axis_size("circ")
    above = lax.ppermute(field[:, -width:, :], "blk", [(i, i + 1) for i in range(rows - 1)])
    below = lax.ppermute(field[:, :width, :], "blk", [(i + 1, i) for i in range(rows - 1)])
    field = jnp.concatenate([above, field, below], axis=1)
    left = lax.ppermute(field[:, :, -width:], "circ", [(i, (i + 1) % cols) for i in range(cols)])
    right = lax.ppermute(field[:, :, :width], "circ", [(i, (i - 1) % cols) for i in range(cols)])
    return jnp.concatenate([left, field, right], axis=2)


def laplace_inner(extended):
    return (
        extended[..., 2:, 1:-1]
        + extended[..., :-2, 1:-1]
        + extended[..., 1:-1, 2:]
        + extended[..., 1:-1, :-2]
        - 4.0 * extended[..., 1:-1, 1:-1]
    )


def trim(field, width):
    return field[..., width:field.shape[-2] - width, width:field.shape[-1] - width]


def kernel_blocks(targets, sources):
    radial = jnp.sqrt(targets[0] * targets[0] + targets[1] * targets[1])
    normal_x = (targets[0] / radial)[:, None]
    normal_y = (targets[1] / radial)[:, None]
    delta_x = targets[0][:, None] - sources[0][None, :]
    delta_y = targets[1][:, None] - sources[1][None, :]
    delta_z = targets[2][:, None] - sources[2][None, :]
    areas = sources[3][None, :]
    dist_sq = delta_x * delta_x + delta_y * delta_y + delta_z * delta_z + areas / math.pi
    distance = jnp.sqrt(dist_sq)
    inverse = 1.0 / distance
    phase_arg = wave_number * distance
    cosine = jnp.cos(phase_arg)
    sine_part = jnp.sin(phase_arg)
    weight = areas * (1.0 / (4.0 * math.pi)) * inverse
    single = single_scale * weight
    double = double_scale * weight * (normal_x * delta_x + normal_y * delta_y) * inverse * inverse
    real_stack = jnp.concatenate(
        [single * cosine, double * (-cosine - phase_arg * sine_part)], axis=0
    )
    imag_stack = jnp.concatenate(
        [single * sine_part, double * (phase_arg * cosine - sine_part)], axis=0
    )
    return (real_stack.astype(jnp.bfloat16), imag_stack.astype(jnp.bfloat16))


def form_kernels(targets, sources):
    width = sources.shape[1]
    block_cols = width
    block_count = width // block_cols
    source_blocks = jnp.transpose(sources.reshape(4, block_count, block_cols), (1, 0, 2))
    real_blocks, imag_blocks = lax.map(lambda block: kernel_blocks(targets, block), source_blocks)
    rows_out = real_blocks.shape[1]
    real_stack = jnp.transpose(real_blocks, (1, 0, 2)).reshape(rows_out, width)
    imag_stack = jnp.transpose(imag_blocks, (1, 0, 2)).reshape(rows_out, width)
    return (real_stack, imag_stack)


def fold_columns(real_stack, imag_stack):

    def fold_step(running, shard_piece, first_col):
        half = shard_piece.shape[0] // 2
        rotated = jnp.concatenate([-shard_piece[half:], shard_piece[:half]], axis=0)
        first = jnp.einsum("lc,rc->lr", shard_piece, real_stack, preferred_element_type=jnp.float32)
        second = jnp.einsum("lc,rc->lr", rotated, imag_stack, preferred_element_type=jnp.float32)
        return first + second

    return fold_step


def relax(motion, bend, load, stiffness, hoop_rows):
    half = motion.shape[0] // 2
    shift = hoop_spring * hoop_rows - inertia_term
    applied_re = bend[:half] - loss_factor * bend[half:] + shift * motion[:half]
    applied_im = bend[half:] + loss_factor * bend[:half] + shift * motion[half:]
    resid_re = load[:half] - applied_re
    resid_im = load[half:] - applied_im
    diag_re = 20.0 * stiffness + shift
    diag_im = 20.0 * loss_factor * stiffness
    denom = diag_re * diag_re + diag_im * diag_im
    update_re = (resid_re * diag_re + resid_im * diag_im) / denom
    update_im = (resid_im * diag_re - resid_re * diag_im) / denom
    return motion + relaxation * jnp.concatenate([update_re, update_im], axis=0)


def per_device(
    panels, node_of_panel, stiffener_rows, density_start, motion_start, force, stiffness
):
    panel_dev = panels.shape[1]
    channels = density_start.shape[0]
    axial, circum = stiffness.shape
    width = 2 * SWEEPS
    blk_index = lax.axis_index("blk")
    devices = lax.axis_size("blk") * lax.axis_size("circ")
    total_rows = axial * lax.axis_size("blk")
    rows_global = blk_index * axial - width + jnp.arange(axial + 2 * width, dtype=jnp.int32)
    inside = ((rows_global >= 0) & (rows_global < total_rows))[:, None]
    hoop_rows = jnp.any(rows_global[:, None] == stiffener_rows[None, :], axis=1).astype(
        jnp.float32
    )[:, None]
    panel_weight = panels[3] * (panel_dev * devices / (8.0 * math.pi))
    joined = gather_columns(jnp.concatenate([panels, density_start], axis=0))
    sources = joined[:4]
    target_rows = panels.shape[1]
    real_stack, imag_stack = form_kernels(panels, sources)
    fold_step = fold_columns(real_stack, imag_stack)
    density = density_start
    motion = motion_start
    pressure = jnp.zeros_like(density_start)
    for round_index in range(ITERS):
        flat_motion = motion.reshape(channels, axial * circum)
        neumann = jnp.take(flat_motion, node_of_panel, axis=1)
        density_bf = density.astype(jnp.bfloat16)
        if round_index == 0:
            gathered = joined[4:].astype(jnp.bfloat16)
        else:
            gathered = gather_columns(density_bf)
        start_sum = jnp.zeros((channels, 2 * target_rows), jnp.float32)
        combined = fold_step(start_sum, gathered, jnp.int32(0))
        single_part = combined[:, :target_rows]
        double_part = combined[:, target_rows:]
        pressure = single_part
        density = 0.5 * density + neumann - double_part
        fluid = jnp.zeros((channels, axial * circum), jnp.float32)
        fluid = fluid.at[:, node_of_panel].add(panel_weight[None, :] * pressure)
        load = force - fluid.reshape(channels, axial, circum)
        state = with_halo(jnp.concatenate([motion, load, stiffness[None]], axis=0), width)
        motion_ext = state[:channels]
        load_ext = state[channels:2 * channels]
        stiff_ext = state[2 * channels]
        for sweep_index in range(SWEEPS):
            edge = 2 * sweep_index + 1
            moment = trim(stiff_ext, edge) * laplace_inner(motion_ext)
            moment = jnp.where(inside[edge:inside.shape[0] - edge], moment, 0.0)
            bend = laplace_inner(moment)
            edge += 1
            rows_at = slice(edge, inside.shape[0] - edge)
            motion_ext = relax(
                trim(motion_ext, 2), bend, trim(load_ext, edge), trim(stiff_ext, edge), hoop_rows[rows_at]
            )
            motion_ext = jnp.where(inside[rows_at], motion_ext, 0.0)
        motion = motion_ext
    return (density, pressure, motion)


def solution(mesh):
    in_specs = (
        P(None, ("blk", "circ")),
        P(("blk", "circ")),
        P(),
        P(None, ("blk", "circ")),
        P(None, "blk", "circ"),
        P(None, "blk", "circ"),
        P("blk", "circ"),
    )
    out_specs = (P(None, ("blk", "circ")), P(None, ("blk", "circ")), P(None, "blk", "circ"))
    return jax.shard_map(
        per_device, mesh=mesh, in_specs=in_specs, out_specs=out_specs, check_vma=False
    )
```
